256 devices in a mesh: blk: 4 (over y_hi, core), reader: 8 (over y_lo, x), bulk: 8 (over z).
Axes of the slice: x: 4, y: 4 (y_hi: 2, y_lo: 2; y = y_hi * 2 + y_lo), z: 8, core: 2. Of those that a mesh axis runs over, the one named last changes fastest.
Arguments:
- vectors: float32 [128, 32768], P('bulk', ('blk', 'reader')), may hold values from -6 to 6
- ham_tiles: float32 [32, 4, 24, 128, 128], P(('blk', 'reader'))
- tile_rows: int32 [32, 4, 24], P(('blk', 'reader')), may hold values from 0 to 7, as said below
- tile_cols: int32 [32, 4, 24], P(('blk', 'reader')), may hold values from 0 to 63
- center: float32 [1], replicated, may hold values from -0.5 to 0.5
- halfwidth: float32 [1], replicated, may hold values from 1 to 2
Outputs:
- filtered: float32 [128, 32768], P('bulk', ('blk', 'reader'))
The draws below stay inside these ranges and needn't reach their ends.
Inputs may be any that keep to these rules, and one draw needn't show every extreme that they name: tile_rows and tile_cols of one panel together name 24 different tiles.
All inputs are finite; a program needn't handle non-finite values.
Results may differ from the reference program's by a relative error of at most 0.0003.
Values sent between devices are 32-bit elements; how exact they have to be, the bound alone decides.
No kernel may reach another device: no remote copies, remote signals or barrier semaphores. Data moves between devices by JAX's collectives and lax.ppermute only.
A program may use at most 64 MiB of HBM per device.

```python
import jax
import jax.numpy as jnp
from jax import lax

VECS = 128
TILE = 128
RT = 8
PT = 24
PASSES = 2
NBLOCKS = 32
NROWS = 32768
N_BLK = 4
N_READER = 8


def pattern_draw(key):
    inner = jax.random.fold_in(key, 7)
    total = N_READER * RT * RT
    panels = NBLOCKS * N_BLK
    keys = jax.random.split(inner, panels)
    perms = jax.vmap(lambda k: jax.random.permutation(k, total))(keys)[:, :PT].astype(jnp.int32)
    panel_ids = jnp.arange(panels, dtype=jnp.int32)
    moved = jnp.where(panel_ids % 2 == 0, total - 1 - perms[:, 0], total - perms[:, 0])
    places = (perms + moved[:, None]) % total
    places = places.reshape(NBLOCKS, N_BLK, PT)
    return (places // (N_READER * RT), places % (N_READER * RT))


def draw_tile_rows(key, part):
    return pattern_draw(key)[0].astype(jnp.int32)


def draw_tile_cols(key, part):
    return pattern_draw(key)[1].astype(jnp.int32)


def draw_ham_tiles(key, part):
    shape = (NBLOCKS, N_BLK, PT, TILE, TILE)
    first = jax.random.fold_in(jax.random.fold_in(key, 11), 0)
    fan = TILE * N_BLK * PT / RT
    rising = 3.0 ** (jnp.arange(NBLOCKS, dtype=jnp.float32) / (NBLOCKS - 1))
    rising = rising.reshape(NBLOCKS, 1, 1, 1, 1)
    base = jax.random.normal(first, shape, jnp.float32)
    return (base * rising / jnp.sqrt(fan)).astype(jnp.float32)


def levels(own_key, dims, shards, least, top_value):
    gain = 1.0
    for dim, shards_of in shards:
        draws = jax.random.uniform(jax.random.fold_in(jax.random.fold_in(own_key, 6), dim), (shards_of,), jnp.float32, least / len(shards), top_value / len(shards))
        gain = gain * jnp.repeat(jnp.exp(draws), dims[dim] // shards_of).reshape((-1,) + (1,) * (len(dims) - 1 - dim))
    return gain


def bell_draw(own_key, extent, scale, bound, shards=(), kind=jnp.bfloat16):
    loudness = levels(own_key, extent, shards, -0.22, 0.18) if shards else 1.0
    array = jax.random.normal(own_key, extent, jnp.float32) * scale * loudness
    return jnp.minimum(jnp.maximum(array, -bound), bound).astype(kind)


def setup_inputs(seed: int = 0) -> dict:
    key_of = jax.random.split(jax.random.key(seed), 7)
    return {
        "vectors": bell_draw(key_of[0], (VECS, NROWS), 1.0, 6.0, ((0, 8), (1, 32)), jnp.float32),
        "ham_tiles": draw_ham_tiles(jax.random.fold_in(key_of[6], 71), 0),
        "tile_rows": draw_tile_rows(jax.random.fold_in(key_of[6], 71), 0),
        "tile_cols": draw_tile_cols(jax.random.fold_in(key_of[6], 71), 0),
        "center": jnp.clip(jax.random.uniform(key_of[4], (1,), jnp.float32, -0.5, 0.5), -0.5, 0.5),
        "halfwidth": jnp.clip(jax.random.uniform(key_of[5], (1,), jnp.float32, 1.0, 2.0), 1.0, 2.0),
    }


def contribute(sources, tiles, rows, count):
    prod = jnp.einsum('vkc,krc->vkr', sources, tiles, precision=lax.Precision.HIGHEST)
    onehot = (rows[:, None] == jnp.arange(count, dtype=jnp.int32)[None, :]).astype(jnp.float32)
    return jnp.einsum('vkr,kt->vtr', prod, onehot, precision=lax.Precision.HIGHEST)

def apply_ham(current, ham_tiles, tile_rows, tile_cols):
    tiled = current.reshape(VECS, NBLOCKS * RT, TILE)
    offsets = (jnp.arange(N_BLK, dtype=jnp.int32) * (N_READER * RT))[:, None]

    def one_block(items):
        tiles, rows, cols = items
        glob = (offsets + cols).reshape(-1).astype(jnp.int32)
        sources = jnp.take(tiled, glob, axis=1)
        return contribute(sources, tiles.reshape(N_BLK * PT, TILE, TILE), rows.reshape(-1), RT)
    blocks = lax.map(one_block, (ham_tiles, tile_rows, tile_cols))
    return jnp.transpose(blocks, (1, 0, 2, 3)).reshape(VECS, NBLOCKS * RT * TILE)

def reference(vectors, ham_tiles, tile_rows, tile_cols, center, halfwidth):

    def scaled(v):
        return (apply_ham(v, ham_tiles, tile_rows, tile_cols) - center[0] * v) / halfwidth[0]
    current = vectors
    for step in range(PASSES):
        first = scaled(current)
        second = 2.0 * scaled(first) - current
        third = 2.0 * scaled(second) - first
        sq = lax.optimization_barrier(jnp.sum(third * third, axis=1))
        current = third / jnp.sqrt(sq / NROWS + 1e-06)[:, None]
    return current
```

```python
import jax
import jax.numpy as jnp
from jax import lax
from jax.sharding import PartitionSpec as P

TILE = 128
PASSES = 2
AXES = ("blk", "reader")
RING = 4


def device_index(core, y, x):
    return ((y // 2) * 2 + core) * 8 + (y % 2) * 4 + x


def shift_perm(step, first_axis_by_core):
    pairs = []
    for core in range(2):
        axis = first_axis_by_core[core]
        for y in range(RING):
            for x in range(RING):
                if axis == "x":
                    dst = device_index(core, y, (x + step) % RING)
                else:
                    dst = device_index(core, (y + step) % RING, x)
                pairs.append((device_index(core, y, x), dst))
    return pairs


def core_swap_perm():
    pairs = []
    for core in range(2):
        for y in range(RING):
            for x in range(RING):
                pairs.append((device_index(core, y, x), device_index(1 - core, y, x)))
    return pairs


def ring_gather(leaves, axis_by_core):
    plus = shift_perm(1, axis_by_core)
    minus = shift_perm(RING - 1, axis_by_core)
    from_left = lax.ppermute(leaves, AXES, plus)
    from_right = lax.ppermute(leaves, AXES, minus)
    half = leaves[0].shape[0] // 2
    far_a = lax.ppermute([l[:half] for l in from_right], AXES, minus)
    far_b = lax.ppermute([l[half:] for l in from_left], AXES, plus)
    out = []
    for own, r, far0, far1, left in zip(leaves, from_right, far_a, far_b, from_left):
        far = jnp.concatenate([far0, far1], axis=0)
        out.append(jnp.stack([own, r, far, left], axis=0))
    return out


def plane_gather(leaves):
    core = lax.axis_index("blk") % 2
    vecs = leaves[0].shape[0]
    hv = vecs // 2
    mine = [lax.dynamic_slice_in_dim(l, core * hv, hv, axis=0) for l in leaves]
    theirs = [lax.dynamic_slice_in_dim(l, (1 - core) * hv, hv, axis=0) for l in leaves]
    got = lax.ppermute(theirs, AXES, core_swap_perm())
    pair = []
    for m, g in zip(mine, got):
        first = jnp.where(core == 0, m, g)
        second = jnp.where(core == 0, g, m)
        pair.append(jnp.stack([first, second], axis=0))
    stage1 = ring_gather(pair, ("x", "y"))
    stage2 = ring_gather(stage1, ("y", "x"))
    other = lax.ppermute(stage2, AXES, core_swap_perm())
    result = []
    for s, o in zip(stage2, other):
        h0 = jnp.where(core == 0, s, o)
        h1 = jnp.where(core == 0, o, s)
        result.append((h0, h1))
    return result


def layout_index(q_index, x0, y0):
    blk = q_index // 8
    reader = q_index % 8
    cc = blk % 2
    y = (blk // 2) * 2 + reader // 4
    x = reader % 4
    dy = (y - y0) % RING
    dx = (x - x0) % RING
    return (dy * 4 + dx) * 2 + cc, (dx * 4 + dy) * 2 + cc


def butterfly_sum(value):
    def partner(flip):
        pairs = []
        for core in range(2):
            for y in range(RING):
                for x in range(RING):
                    c2, y2, x2 = core, y, x
                    if flip == "core":
                        c2 = 1 - core
                    elif flip == "y1":
                        y2 = y ^ 1
                    elif flip == "y2":
                        y2 = y ^ 2
                    elif flip == "x1":
                        x2 = x ^ 1
                    else:
                        x2 = x ^ 2
                    pairs.append((device_index(core, y, x), device_index(c2, y2, x2)))
        return pairs

    for flip in ("core", "y1", "x1", "y2", "x2"):
        value = value + lax.ppermute(value, AXES, partner(flip))
    return value


def shards(vectors, ham_tiles, tile_rows, tile_cols, center, halfwidth):
    tiles_here = ham_tiles[0]
    rows_here = tile_rows[0]
    cols_here = tile_cols[0]
    vecs = vectors.shape[0]
    hv = vecs // 2
    width = vectors.shape[1]
    row_tiles = width // TILE
    groups = tiles_here.shape[0]
    slots = tiles_here.shape[1]
    nblocks = lax.axis_size("blk") * lax.axis_size("reader")
    total_rows = width * nblocks
    group_tiles = lax.axis_size("reader") * row_tiles

    reader = lax.axis_index("reader")
    blk = lax.axis_index("blk")
    x0 = reader % 4
    y0 = (blk // 2) * 2 + reader // 4

    offsets = (jnp.arange(groups, dtype=jnp.int32) * group_tiles)[:, None]
    glob = (offsets + cols_here).reshape(-1)
    q_of = glob // row_tiles
    t_of = glob % row_tiles
    b0, b1 = layout_index(q_of, x0, y0)
    all_q = jnp.arange(nblocks, dtype=jnp.int32)
    p0, p1 = layout_index(all_q, x0, y0)

    tiles = tiles_here.reshape(groups * slots, TILE, TILE)
    rows = rows_here.reshape(-1)
    onehot = (rows[:, None] == jnp.arange(row_tiles, dtype=jnp.int32)[None, :]).astype(jnp.float32)

    def sources_of(h0, h1):
        f0 = h0.reshape(nblocks, hv, row_tiles, TILE)
        f1 = h1.reshape(nblocks, hv, row_tiles, TILE)
        s0 = f0[b0, :, t_of, :]
        s1 = f1[b1, :, t_of, :]
        return jnp.concatenate([s0, s1], axis=1)

    def apply_sources(sources):
        product = jnp.einsum("kvc,krc->kvr", sources, tiles, precision=lax.Precision.HIGHEST)
        total = jnp.einsum("kvr,kt->vtr", product, onehot, precision=lax.Precision.HIGHEST)
        return total.reshape(vecs, width)

    def scaled(field):
        ((h0, h1),) = plane_gather([field])
        out = apply_sources(sources_of(h0, h1))
        return (out - center[0] * field) / halfwidth[0]

    current = vectors
    third = None
    partial = None
    for step in range(PASSES):
        if step == 0:
            first = scaled(current)
        else:
            (h0, h1), (s0, s1) = plane_gather([third, partial])
            sq0 = s0.reshape(nblocks, hv)[p0]
            sq1 = s1.reshape(nblocks, hv)[p1]
            squares = jnp.sum(jnp.concatenate([sq0, sq1], axis=1), axis=0)
            norm = jnp.sqrt(squares / total_rows + 1e-06)
            current = third / norm[:, None]
            sources = sources_of(h0, h1) / norm[None, :, None]
            first = (apply_sources(sources) - center[0] * current) / halfwidth[0]
        second = 2.0 * scaled(first) - current
        third = 2.0 * scaled(second) - first
        partial = jnp.sum(third * third, axis=1)[:, None]
    squares = butterfly_sum(partial[:, 0])
    return third / jnp.sqrt(squares / total_rows + 1e-06)[:, None]


def solution(mesh):
    return jax.shard_map(
        shards,
        mesh=mesh,
        in_specs=(
            P("bulk", ("blk", "reader")),
            P(("blk", "reader"), None, None, None, None),
            P(("blk", "reader"), None, None),
            P(("blk", "reader"), None, None),
            P(),
            P(),
        ),
        out_specs=P("bulk", ("blk", "reader")),
        check_vma=False,
    )
```

```python
import jax
import jax.numpy as jnp
from jax import lax
from jax.sharding import PartitionSpec as P

TILE = 128
PASSES = 2
AXES = ("blk", "reader")
RING = 4


def device_index(core, y, x):
    return ((y // 2) * 2 + core) * 8 + (y % 2) * 4 + x


def shift_perm(step, first_axis_by_core):
    pairs = []
    for core in range(2):
        axis = first_axis_by_core[core]
        for y in range(RING):
            for x in range(RING):
                if axis == "x":
                    dst = device_index(core, y, (x + step) % RING)
                else:
                    dst = device_index(core, (y + step) % RING, x)
                pairs.append((device_index(core, y, x), dst))
    return pairs


def core_swap_perm():
    pairs = []
    for core in range(2):
        for y in range(RING):
            for x in range(RING):
                pairs.append((device_index(core, y, x), device_index(1 - core, y, x)))
    return pairs


def ring_gather(leaves, axis_by_core):
    plus = shift_perm(1, axis_by_core)
    minus = shift_perm(RING - 1, axis_by_core)
    from_left = lax.ppermute(leaves, AXES, plus)
    from_right = lax.ppermute(leaves, AXES, minus)
    half = leaves[0].shape[0] // 2
    far_a = lax.ppermute([l[:half] for l in from_right], AXES, minus)
    far_b = lax.ppermute([l[half:] for l in from_left], AXES, plus)
    out = []
    for own, r, far0, far1, left in zip(leaves, from_right, far_a, far_b, from_left):
        far = jnp.concatenate([far0, far1], axis=0)
        out.append(jnp.stack([own, r, far, left], axis=0))
    return out


def plane_gather(leaves):
    core = lax.axis_index("blk") % 2
    vecs = leaves[0].shape[0]
    hv = vecs // 2
    mine = [lax.dynamic_slice_in_dim(l, core * hv, hv, axis=0) for l in leaves]
    theirs = [lax.dynamic_slice_in_dim(l, (1 - core) * hv, hv, axis=0) for l in leaves]
    got = lax.ppermute(theirs, AXES, core_swap_perm())
    pair = []
    for m, g in zip(mine, got):
        first = jnp.where(core == 0, m, g)
        second = jnp.where(core == 0, g, m)
        pair.append(jnp.stack([first, second], axis=0))
    stage1 = ring_gather(pair, ("x", "y"))
    stage2 = ring_gather(stage1, ("y", "x"))
    other = lax.ppermute(stage2, AXES, core_swap_perm())
    result = []
    for s, o in zip(stage2, other):
        h0 = jnp.where(core == 0, s, o)
        h1 = jnp.where(core == 0, o, s)
        result.append((h0, h1))
    return result


def layout_index(q_index, x0, y0):
    blk = q_index // 8
    reader = q_index % 8
    cc = blk % 2
    y = (blk // 2) * 2 + reader // 4
    x = reader % 4
    dy = (y - y0) % RING
    dx = (x - x0) % RING
    return (dy * 4 + dx) * 2 + cc, (dx * 4 + dy) * 2 + cc


def butterfly_sum(value):
    def partner(flip):
        pairs = []
        for core in range(2):
            for y in range(RING):
                for x in range(RING):
                    c2, y2, x2 = core, y, x
                    if flip == "core":
                        c2 = 1 - core
                    elif flip == "y1":
                        y2 = y ^ 1
                    elif flip == "y2":
                        y2 = y ^ 2
                    elif flip == "x1":
                        x2 = x ^ 1
                    else:
                        x2 = x ^ 2
                    pairs.append((device_index(core, y, x), device_index(c2, y2, x2)))
        return pairs

    for flip in ("core", "y1", "x1", "y2", "x2"):
        value = value + lax.ppermute(value, AXES, partner(flip))
    return value


def shards(vectors, ham_tiles, tile_rows, tile_cols, center, halfwidth):
    tiles_here = ham_tiles[0]
    rows_here = tile_rows[0]
    cols_here = tile_cols[0]
    vecs = vectors.shape[0]
    hv = vecs // 2
    width = vectors.shape[1]
    row_tiles = width // TILE
    groups = tiles_here.shape[0]
    slots = tiles_here.shape[1]
    nblocks = lax.axis_size("blk") * lax.axis_size("reader")
    total_rows = width * nblocks
    group_tiles = lax.axis_size("reader") * row_tiles

    reader = lax.axis_index("reader")
    blk = lax.axis_index("blk")
    x0 = reader % 4
    y0 = (blk // 2) * 2 + reader // 4

    offsets = (jnp.arange(groups, dtype=jnp.int32) * group_tiles)[:, None]
    glob = (offsets + cols_here).reshape(-1)
    q_of = glob // row_tiles
    t_of = glob % row_tiles
    b0, b1 = layout_index(q_of, x0, y0)
    all_q = jnp.arange(nblocks, dtype=jnp.int32)
    p0, p1 = layout_index(all_q, x0, y0)

    tiles = tiles_here.reshape(groups * slots, TILE, TILE)
    rows = rows_here.reshape(-1)
    onehot = (rows[:, None] == jnp.arange(row_tiles, dtype=jnp.int32)[None, :]).astype(jnp.float32)

    def sources_of(h0, h1):
        f0 = h0.reshape(nblocks, hv, row_tiles, TILE)
        f1 = h1.reshape(nblocks, hv, row_tiles, TILE)
        s0 = f0[b0, :, t_of, :]
        s1 = f1[b1, :, t_of, :]
        return jnp.concatenate([s0, s1], axis=1)

    def apply_sources(sources):
        product = jnp.einsum("kvc,krc->kvr", sources, tiles, precision=lax.Precision.HIGH)
        total = jnp.einsum("kvr,kt->vtr", product, onehot, precision=lax.Precision.HIGHEST)
        return total.reshape(vecs, width)

    def scaled(field):
        ((h0, h1),) = plane_gather([field])
        out = apply_sources(sources_of(h0, h1))
        return (out - center[0] * field) / halfwidth[0]

    current = vectors
    third = None
    partial = None
    for step in range(PASSES):
        if step == 0:
            first = scaled(current)
        else:
            (h0, h1), (s0, s1) = plane_gather([third, partial])
            sq0 = s0.reshape(nblocks, hv)[p0]
            sq1 = s1.reshape(nblocks, hv)[p1]
            squares = jnp.sum(jnp.concatenate([sq0, sq1], axis=1), axis=0)
            norm = jnp.sqrt(squares / total_rows + 1e-06)
            current = third / norm[:, None]
            sources = sources_of(h0, h1) / norm[None, :, None]
            first = (apply_sources(sources) - center[0] * current) / halfwidth[0]
        second = 2.0 * scaled(first) - current
        third = 2.0 * scaled(second) - first
        partial = jnp.sum(third * third, axis=1)[:, None]
    squares = butterfly_sum(partial[:, 0])
    return third / jnp.sqrt(squares / total_rows + 1e-06)[:, None]


def solution(mesh):
    return jax.shard_map(
        shards,
        mesh=mesh,
        in_specs=(
            P("bulk", ("blk", "reader")),
            P(("blk", "reader"), None, None, None, None),
            P(("blk", "reader"), None, None),
            P(("blk", "reader"), None, None),
            P(),
            P(),
        ),
        out_specs=P("bulk", ("blk", "reader")),
        check_vma=False,
    )
```

```python
import jax
import jax.numpy as jnp
from jax import lax
from jax.sharding import PartitionSpec as P

TILE = 128
PASSES = 2
AXES = ("blk", "reader")
RING = 4


def device_index(core, y, x):
    return ((y // 2) * 2 + core) * 8 + (y % 2) * 4 + x


def shift_perm(step, first_axis_by_core):
    pairs = []
    for core in range(2):
        axis = first_axis_by_core[core]
        for y in range(RING):
            for x in range(RING):
                if axis == "x":
                    dst = device_index(core, y, (x + step) % RING)
                else:
                    dst = device_index(core, (y + step) % RING, x)
                pairs.append((device_index(core, y, x), dst))
    return pairs


def core_swap_perm():
    pairs = []
    for core in range(2):
        for y in range(RING):
            for x in range(RING):
                pairs.append((device_index(core, y, x), device_index(1 - core, y, x)))
    return pairs


def direct_round(leaves, axis_by_core):
    got = [lax.ppermute(leaves, AXES, shift_perm(RING - step, axis_by_core)) for step in (1, 2, 3)]
    return [jnp.stack([own, a, b, c], axis=0) for own, a, b, c in zip(leaves, *got)]


def plane_gather(leaves):
    stage1 = direct_round(leaves, ("x", "y"))
    stage2 = direct_round(stage1, ("y", "x"))
    other = lax.ppermute(stage2, AXES, core_swap_perm())
    out = []
    for s, o in zip(stage2, other):
        both = jnp.concatenate([s.reshape((RING * RING,) + s.shape[2:]), o.reshape((RING * RING,) + o.shape[2:])], axis=0)
        out.append(both)
    return out


def layout_index(q_index, x0, y0, core):
    blk = q_index // 8
    reader = q_index % 8
    cc = blk % 2
    y = (blk // 2) * 2 + reader // 4
    x = reader % 4
    dy = (y - y0) % RING
    dx = (x - x0) % RING
    chip = jnp.where(cc == 0, dy * 4 + dx, dx * 4 + dy)
    return jnp.where(cc == core, 0, RING * RING) + chip


def shards(vectors, ham_tiles, tile_rows, tile_cols, center, halfwidth):
    tiles_here = ham_tiles[0]
    rows_here = tile_rows[0]
    cols_here = tile_cols[0]
    vecs = vectors.shape[0]
    width = vectors.shape[1]
    row_tiles = width // TILE
    groups = tiles_here.shape[0]
    slots = tiles_here.shape[1]
    nblocks = lax.axis_size("blk") * lax.axis_size("reader")
    total_rows = width * nblocks
    group_tiles = lax.axis_size("reader") * row_tiles

    reader = lax.axis_index("reader")
    blk = lax.axis_index("blk")
    x0 = reader % 4
    y0 = (blk // 2) * 2 + reader // 4

    offsets = (jnp.arange(groups, dtype=jnp.int32) * group_tiles)[:, None]
    glob = (offsets + cols_here).reshape(-1)
    q_of = glob // row_tiles
    t_of = glob % row_tiles
    core = blk % 2
    b_of = layout_index(q_of, x0, y0, core)
    all_q = jnp.arange(nblocks, dtype=jnp.int32)
    p_of = layout_index(all_q, x0, y0, core)

    tiles = tiles_here.reshape(groups * slots, TILE, TILE)
    rows = rows_here.reshape(-1)
    onehot = (rows[:, None] == jnp.arange(row_tiles, dtype=jnp.int32)[None, :]).astype(jnp.float32)

    def sources_of(gathered):
        f = gathered.reshape(nblocks, vecs, row_tiles, TILE)
        return f[b_of, :, t_of, :]

    def total_squares(gathered):
        return jnp.sum(gathered.reshape(nblocks, vecs)[p_of], axis=0)

    def apply_sources(sources):
        product = jnp.einsum("kvc,krc->kvr", sources, tiles, precision=lax.Precision.HIGH)
        total = jnp.einsum("kvr,kt->vtr", product, onehot, precision=lax.Precision.HIGHEST)
        return total.reshape(vecs, width)

    def scaled(field):
        (gathered,) = plane_gather([field])
        out = apply_sources(sources_of(gathered))
        return (out - center[0] * field) / halfwidth[0]

    current = vectors
    third = None
    partial = None
    for step in range(PASSES):
        if step == 0:
            first = scaled(current)
        else:
            gathered, sq = plane_gather([third, partial])
            squares = total_squares(sq)
            norm = jnp.sqrt(squares / total_rows + 1e-06)
            current = third / norm[:, None]
            sources = sources_of(gathered) / norm[None, :, None]
            first = (apply_sources(sources) - center[0] * current) / halfwidth[0]
        second = 2.0 * scaled(first) - current
        third = 2.0 * scaled(second) - first
        partial = jnp.sum(third * third, axis=1)[:, None]
    (sq,) = plane_gather([partial])
    squares = total_squares(sq)
    return third / jnp.sqrt(squares / total_rows + 1e-06)[:, None]


def solution(mesh):
    return jax.shard_map(
        shards,
        mesh=mesh,
        in_specs=(
            P("bulk", ("blk", "reader")),
            P(("blk", "reader"), None, None, None, None),
            P(("blk", "reader"), None, None),
            P(("blk", "reader"), None, None),
            P(),
            P(),
        ),
        out_specs=P("bulk", ("blk", "reader")),
        check_vma=False,
    )
```

```python
import jax
import jax.numpy as jnp
from jax import lax
from jax.sharding import PartitionSpec as P

TILE = 128
PASSES = 2
AXES = ("blk", "reader")
RING = 4


def device_index(core, y, x):
    return ((y // 2) * 2 + core) * 8 + (y % 2) * 4 + x


def shift_perm(step, first_axis_by_core):
    pairs = []
    for core in range(2):
        axis = first_axis_by_core[core]
        for y in range(RING):
            for x in range(RING):
                if axis == "x":
                    dst = device_index(core, y, (x + step) % RING)
                else:
                    dst = device_index(core, (y + step) % RING, x)
                pairs.append((device_index(core, y, x), dst))
    return pairs


def core_swap_perm():
    pairs = []
    for core in range(2):
        for y in range(RING):
            for x in range(RING):
                pairs.append((device_index(core, y, x), device_index(1 - core, y, x)))
    return pairs


def direct_round(leaves, axis_by_core):
    got = [lax.ppermute(leaves, AXES, shift_perm(RING - step, axis_by_core)) for step in (1, 2, 3)]
    return [jnp.stack([own, a, b, c], axis=0) for own, a, b, c in zip(leaves, *got)]


def plane_gather(leaves):
    stage1 = direct_round(leaves, ("x", "y"))
    stage2 = direct_round(stage1, ("y", "x"))
    other = lax.ppermute(stage2, AXES, core_swap_perm())
    out = []
    for s, o in zip(stage2, other):
        both = jnp.concatenate([s.reshape((RING * RING,) + s.shape[2:]), o.reshape((RING * RING,) + o.shape[2:])], axis=0)
        out.append(both)
    return out


def layout_index(q_index, x0, y0, core):
    blk = q_index // 8
    reader = q_index % 8
    cc = blk % 2
    y = (blk // 2) * 2 + reader // 4
    x = reader % 4
    dy = (y - y0) % RING
    dx = (x - x0) % RING
    chip = jnp.where(cc == 0, dy * 4 + dx, dx * 4 + dy)
    return jnp.where(cc == core, 0, RING * RING) + chip


def stream(vectors, ham_tiles, tile_rows, tile_cols, center, halfwidth):
    tiles_here = ham_tiles[0]
    rows_here = tile_rows[0]
    cols_here = tile_cols[0]
    vecs = vectors.shape[0]
    width = vectors.shape[1]
    row_tiles = width // TILE
    groups = tiles_here.shape[0]
    slots = tiles_here.shape[1]
    nblocks = lax.axis_size("blk") * lax.axis_size("reader")
    total_rows = width * nblocks
    group_tiles = lax.axis_size("reader") * row_tiles

    reader = lax.axis_index("reader")
    blk = lax.axis_index("blk")
    x0 = reader % 4
    y0 = (blk // 2) * 2 + reader // 4

    offsets = (jnp.arange(groups, dtype=jnp.int32) * group_tiles)[:, None]
    glob = (offsets + cols_here).reshape(-1)
    q_of = glob // row_tiles
    t_of = glob % row_tiles
    core = blk % 2
    b_of = layout_index(q_of, x0, y0, core)
    all_q = jnp.arange(nblocks, dtype=jnp.int32)
    p_of = layout_index(all_q, x0, y0, core)

    tiles = tiles_here.reshape(groups * slots, TILE, TILE)
    rows = rows_here.reshape(-1)
    onehot = (rows[:, None] == jnp.arange(row_tiles, dtype=jnp.int32)[None, :]).astype(jnp.float32)

    def sources_of(gathered):
        f = gathered.reshape(nblocks, vecs, row_tiles, TILE)
        return f[b_of, :, t_of, :]

    def total_squares(gathered):
        return jnp.sum(gathered.reshape(nblocks, vecs)[p_of], axis=0)

    def apply_sources(sources):
        product = jnp.einsum("kvc,krc->kvr", sources, tiles, precision=lax.Precision.HIGH)
        total = jnp.einsum("kvr,kt->vtr", product, onehot, precision=lax.Precision.HIGHEST)
        return total.reshape(vecs, width)

    def scaled(field):
        (gathered,) = plane_gather([field])
        out = apply_sources(sources_of(gathered))
        return (out - center[0] * field) / halfwidth[0]

    current = vectors
    third = None
    partial = None
    for step in range(PASSES):
        if step == 0:
            first = scaled(current)
        else:
            gathered, sq = plane_gather([third, partial])
            squares = total_squares(sq)
            norm = jnp.sqrt(squares / total_rows + 1e-06)
            current = third / norm[:, None]
            sources = sources_of(gathered) / norm[None, :, None]
            first = (apply_sources(sources) - center[0] * current) / halfwidth[0]
        second = 2.0 * scaled(first) - current
        third = 2.0 * scaled(second) - first
        partial = jnp.sum(third * third, axis=1)[:, None]
    (sq,) = plane_gather([partial])
    squares = total_squares(sq)
    return third / jnp.sqrt(squares / total_rows + 1e-06)[:, None]


STREAMS = 2


def shards(vectors, ham_tiles, tile_rows, tile_cols, center, halfwidth):
    parts = jnp.split(vectors, STREAMS, axis=0)
    outs = [stream(p, ham_tiles, tile_rows, tile_cols, center, halfwidth) for p in parts]
    return jnp.concatenate(outs, axis=0)

def solution(mesh):
    return jax.shard_map(
        shards,
        mesh=mesh,
        in_specs=(
            P("bulk", ("blk", "reader")),
            P(("blk", "reader"), None, None, None, None),
            P(("blk", "reader"), None, None),
            P(("blk", "reader"), None, None),
            P(),
            P(),
        ),
        out_specs=P("bulk", ("blk", "reader")),
        check_vma=False,
    )
```

```python
import jax
import jax.numpy as jnp
from jax import lax
from jax.sharding import PartitionSpec as P

TILE = 128
PASSES = 2
AXES = ("blk", "reader")
RING = 4


def device_index(core, y, x):
    return ((y // 2) * 2 + core) * 8 + (y % 2) * 4 + x


def shift_perm(step, first_axis_by_core):
    pairs = []
    for core in range(2):
        axis = first_axis_by_core[core]
        for y in range(RING):
            for x in range(RING):
                if axis == "x":
                    dst = device_index(core, y, (x + step) % RING)
                else:
                    dst = device_index(core, (y + step) % RING, x)
                pairs.append((device_index(core, y, x), dst))
    return pairs


def core_swap_perm():
    pairs = []
    for core in range(2):
        for y in range(RING):
            for x in range(RING):
                pairs.append((device_index(core, y, x), device_index(1 - core, y, x)))
    return pairs


def direct_round(leaves, axis_by_core):
    got = [lax.ppermute(leaves, AXES, shift_perm(RING - step, axis_by_core)) for step in (1, 2, 3)]
    return [jnp.stack([own, a, b, c], axis=0) for own, a, b, c in zip(leaves, *got)]


def plane_gather(leaves):
    stage1 = direct_round(leaves, ("x", "y"))
    stage2 = direct_round(stage1, ("y", "x"))
    other = lax.ppermute(stage2, AXES, core_swap_perm())
    out = []
    for s, o in zip(stage2, other):
        out.append((s.reshape((RING * RING,) + s.shape[2:]), o.reshape((RING * RING,) + o.shape[2:])))
    return out


def layout_index(q_index, x0, y0, core):
    blk = q_index // 8
    reader = q_index % 8
    cc = blk % 2
    y = (blk // 2) * 2 + reader // 4
    x = reader % 4
    dy = (y - y0) % RING
    dx = (x - x0) % RING
    chip = jnp.where(cc == 0, dy * 4 + dx, dx * 4 + dy)
    return jnp.where(cc == core, 0, RING * RING) + chip


def shards(vectors, ham_tiles, tile_rows, tile_cols, center, halfwidth):
    tiles_here = ham_tiles[0]
    rows_here = tile_rows[0]
    cols_here = tile_cols[0]
    vecs = vectors.shape[0]
    width = vectors.shape[1]
    row_tiles = width // TILE
    groups = tiles_here.shape[0]
    slots = tiles_here.shape[1]
    nblocks = lax.axis_size("blk") * lax.axis_size("reader")
    total_rows = width * nblocks
    group_tiles = lax.axis_size("reader") * row_tiles

    reader = lax.axis_index("reader")
    blk = lax.axis_index("blk")
    x0 = reader % 4
    y0 = (blk // 2) * 2 + reader // 4

    core = blk % 2
    all_q = jnp.arange(nblocks, dtype=jnp.int32)
    p_of = layout_index(all_q, x0, y0, core)
    chips = RING * RING

    def split_groups(parity):
        sel = jnp.arange(0, groups, 2, dtype=jnp.int32) + parity
        glob = (sel[:, None] * group_tiles + cols_here[sel]).reshape(-1)
        chip = layout_index(glob // row_tiles, x0, y0, core) % chips
        tiles = tiles_here[sel].reshape(-1, TILE, TILE)
        rows = rows_here[sel].reshape(-1)
        onehot = (rows[:, None] == jnp.arange(row_tiles, dtype=jnp.int32)[None, :]).astype(jnp.float32)
        return chip, glob % row_tiles, tiles, onehot

    own_part = split_groups(core)
    other_part = split_groups(1 - core)

    def sources_of(gathered, part):
        f = gathered.reshape(chips, vecs, row_tiles, TILE)
        return f[part[0], :, part[1], :]

    def total_squares(own_sq, other_sq):
        both = jnp.concatenate([own_sq, other_sq], axis=0)
        return jnp.sum(both.reshape(nblocks, vecs)[p_of], axis=0)

    def apply_part(sources, part):
        product = jnp.einsum("kvc,krc->kvr", sources, part[2], precision=lax.Precision.HIGH)
        return jnp.einsum("kvr,kt->vtr", product, part[3], precision=lax.Precision.HIGHEST)

    def apply_both(own, other, norm=None):
        s_own = sources_of(own, own_part)
        s_other = sources_of(other, other_part)
        if norm is not None:
            s_own = s_own / norm[None, :, None]
            s_other = s_other / norm[None, :, None]
        total = apply_part(s_own, own_part) + apply_part(s_other, other_part)
        return total.reshape(vecs, width)

    def scaled(field):
        ((own, other),) = plane_gather([field])
        out = apply_both(own, other)
        return (out - center[0] * field) / halfwidth[0]

    current = vectors
    third = None
    partial = None
    for step in range(PASSES):
        if step == 0:
            first = scaled(current)
        else:
            (own, other), (own_sq, other_sq) = plane_gather([third, partial])
            squares = total_squares(own_sq, other_sq)
            norm = jnp.sqrt(squares / total_rows + 1e-06)
            current = third / norm[:, None]
            first = (apply_both(own, other, norm) - center[0] * current) / halfwidth[0]
        second = 2.0 * scaled(first) - current
        third = 2.0 * scaled(second) - first
        partial = jnp.sum(third * third, axis=1)[:, None]
    ((own_sq, other_sq),) = plane_gather([partial])
    squares = total_squares(own_sq, other_sq)
    return third / jnp.sqrt(squares / total_rows + 1e-06)[:, None]


def solution(mesh):
    return jax.shard_map(
        shards,
        mesh=mesh,
        in_specs=(
            P("bulk", ("blk", "reader")),
            P(("blk", "reader"), None, None, None, None),
            P(("blk", "reader"), None, None),
            P(("blk", "reader"), None, None),
            P(),
            P(),
        ),
        out_specs=P("bulk", ("blk", "reader")),
        check_vma=False,
    )
```

```python
import jax
import jax.numpy as jnp
from jax import lax
from jax.sharding import PartitionSpec as P

TILE = 128
PASSES = 2
AXES = ("blk", "reader")
RING = 4


def device_index(core, y, x):
    return ((y // 2) * 2 + core) * 8 + (y % 2) * 4 + x


def shift_perm(step, first_axis_by_core):
    pairs = []
    for core in range(2):
        axis = first_axis_by_core[core]
        for y in range(RING):
            for x in range(RING):
                if axis == "x":
                    dst = device_index(core, y, (x + step) % RING)
                else:
                    dst = device_index(core, (y + step) % RING, x)
                pairs.append((device_index(core, y, x), dst))
    return pairs


def core_swap_perm():
    pairs = []
    for core in range(2):
        for y in range(RING):
            for x in range(RING):
                pairs.append((device_index(core, y, x), device_index(1 - core, y, x)))
    return pairs


def direct_round(leaves, axis_by_core):
    got = [lax.ppermute(leaves, AXES, shift_perm(RING - step, axis_by_core)) for step in (1, 2, 3)]
    return [jnp.stack([own, a, b, c], axis=0) for own, a, b, c in zip(leaves, *got)]


def plane_gather(leaves):
    stage1 = direct_round(leaves, ("x", "y"))
    stage2 = direct_round(stage1, ("y", "x"))
    other = lax.ppermute(stage2, AXES, core_swap_perm())
    out = []
    for s, o in zip(stage2, other):
        both = jnp.concatenate([s.reshape((RING * RING,) + s.shape[2:]), o.reshape((RING * RING,) + o.shape[2:])], axis=0)
        out.append(both)
    return out


def layout_index(q_index, x0, y0, core):
    blk = q_index // 8
    reader = q_index % 8
    cc = blk % 2
    y = (blk // 2) * 2 + reader // 4
    x = reader % 4
    dy = (y - y0) % RING
    dx = (x - x0) % RING
    chip = jnp.where(cc == 0, dy * 4 + dx, dx * 4 + dy)
    return jnp.where(cc == core, 0, RING * RING) + chip


def shards(vectors, ham_tiles, tile_rows, tile_cols, center, halfwidth):
    tiles_here = ham_tiles[0]
    rows_here = tile_rows[0]
    cols_here = tile_cols[0]
    vecs = vectors.shape[0]
    width = vectors.shape[1]
    row_tiles = width // TILE
    groups = tiles_here.shape[0]
    slots = tiles_here.shape[1]
    nblocks = lax.axis_size("blk") * lax.axis_size("reader")
    total_rows = width * nblocks
    group_tiles = lax.axis_size("reader") * row_tiles

    reader = lax.axis_index("reader")
    blk = lax.axis_index("blk")
    x0 = reader % 4
    y0 = (blk // 2) * 2 + reader // 4

    offsets = (jnp.arange(groups, dtype=jnp.int32) * group_tiles)[:, None]
    glob = (offsets + cols_here).reshape(-1)
    q_of = glob // row_tiles
    t_of = glob % row_tiles
    core = blk % 2
    b_of = layout_index(q_of, x0, y0, core)
    all_q = jnp.arange(nblocks, dtype=jnp.int32)
    p_of = layout_index(all_q, x0, y0, core)

    tiles = tiles_here.reshape(groups * slots, TILE, TILE)
    rows = rows_here.reshape(-1)
    onehot = (rows[:, None] == jnp.arange(row_tiles, dtype=jnp.int32)[None, :]).astype(jnp.float32)

    def sources_of(gathered):
        f = gathered.reshape(nblocks, vecs, row_tiles, TILE)
        return f[b_of, :, t_of, :]

    def total_squares(gathered):
        return jnp.sum(gathered.reshape(nblocks, vecs)[p_of], axis=0)

    def apply_sources(sources):
        product = jnp.einsum("kvc,krc->kvr", sources, tiles, precision=lax.Precision.HIGH)
        total = jnp.einsum("kvr,kt->vtr", product, onehot, precision=lax.Precision.HIGHEST)
        return total.reshape(vecs, width)

    def scaled(field):
        (gathered,) = plane_gather([field])
        out = apply_sources(sources_of(gathered))
        return (out - center[0] * field) / halfwidth[0]

    def one_pass(step, carry):
        third, partial = carry
        gathered, sq = plane_gather([third, partial])
        squares = total_squares(sq)
        norm = jnp.where(step == 0, 1.0, jnp.sqrt(squares / total_rows + 1e-06))
        current = third / norm[:, None]
        sources = sources_of(gathered) / norm[None, :, None]
        first = (apply_sources(sources) - center[0] * current) / halfwidth[0]
        second = 2.0 * scaled(first) - current
        third = 2.0 * scaled(second) - first
        return third, jnp.sum(third * third, axis=1)[:, None]

    start = (vectors, jnp.zeros((vecs, 1), jnp.float32))
    third, partial = lax.fori_loop(0, PASSES, one_pass, start)
    (sq,) = plane_gather([partial])
    squares = total_squares(sq)
    return third / jnp.sqrt(squares / total_rows + 1e-06)[:, None]


def solution(mesh):
    return jax.shard_map(
        shards,
        mesh=mesh,
        in_specs=(
            P("bulk", ("blk", "reader")),
            P(("blk", "reader"), None, None, None, None),
            P(("blk", "reader"), None, None),
            P(("blk", "reader"), None, None),
            P(),
            P(),
        ),
        out_specs=P("bulk", ("blk", "reader")),
        check_vma=False,
    )
```

```python
import jax
import jax.numpy as jnp
from jax import lax
from jax.sharding import PartitionSpec as P

TILE = 128
PASSES = 2
AXES = ("blk", "reader")
RING = 4


def device_index(core, y, x):
    return ((y // 2) * 2 + core) * 8 + (y % 2) * 4 + x


def shift_perm(step, first_axis_by_core):
    pairs = []
    for core in range(2):
        axis = first_axis_by_core[core]
        for y in range(RING):
            for x in range(RING):
                if axis == "x":
                    dst = device_index(core, y, (x + step) % RING)
                else:
                    dst = device_index(core, (y + step) % RING, x)
                pairs.append((device_index(core, y, x), dst))
    return pairs


def core_swap_perm():
    pairs = []
    for core in range(2):
        for y in range(RING):
            for x in range(RING):
                pairs.append((device_index(core, y, x), device_index(1 - core, y, x)))
    return pairs


def direct_round(leaves, axis_by_core):
    got = [lax.ppermute(leaves, AXES, shift_perm(RING - step, axis_by_core)) for step in (1, 2, 3)]
    return [jnp.stack([own, a, b, c], axis=0) for own, a, b, c in zip(leaves, *got)]


def plane_gather(leaves):
    stage1 = direct_round(leaves, ("x", "y"))
    stage2 = direct_round(stage1, ("y", "x"))
    other = lax.ppermute(stage2, AXES, core_swap_perm())
    out = []
    for s, o in zip(stage2, other):
        both = jnp.concatenate([s.reshape((RING * RING,) + s.shape[2:]), o.reshape((RING * RING,) + o.shape[2:])], axis=0)
        out.append(both)
    return out


def layout_index(q_index, x0, y0, core):
    blk = q_index // 8
    reader = q_index % 8
    cc = blk % 2
    y = (blk // 2) * 2 + reader // 4
    x = reader % 4
    dy = (y - y0) % RING
    dx = (x - x0) % RING
    chip = jnp.where(cc == 0, dy * 4 + dx, dx * 4 + dy)
    return jnp.where(cc == core, 0, RING * RING) + chip


def shards(vectors, ham_tiles, tile_rows, tile_cols, center, halfwidth):
    tiles_here = ham_tiles[0]
    rows_here = tile_rows[0]
    cols_here = tile_cols[0]
    vecs = vectors.shape[0]
    width = vectors.shape[1]
    row_tiles = width // TILE
    groups = tiles_here.shape[0]
    slots = tiles_here.shape[1]
    nblocks = lax.axis_size("blk") * lax.axis_size("reader")
    total_rows = width * nblocks
    group_tiles = lax.axis_size("reader") * row_tiles

    reader = lax.axis_index("reader")
    blk = lax.axis_index("blk")
    x0 = reader % 4
    y0 = (blk // 2) * 2 + reader // 4

    offsets = (jnp.arange(groups, dtype=jnp.int32) * group_tiles)[:, None]
    glob = (offsets + cols_here).reshape(-1)
    q_of = glob // row_tiles
    t_of = glob % row_tiles
    core = blk % 2
    b_of = layout_index(q_of, x0, y0, core)
    all_q = jnp.arange(nblocks, dtype=jnp.int32)
    p_of = layout_index(all_q, x0, y0, core)

    tiles = tiles_here.reshape(groups * slots, TILE, TILE)
    tiles_hi_f = lax.reduce_precision(tiles, exponent_bits=8, mantissa_bits=7)
    tiles_hi = tiles_hi_f.astype(jnp.bfloat16)
    tiles_lo = (tiles - tiles_hi_f).astype(jnp.bfloat16)
    rows = rows_here.reshape(-1)
    onehot = (rows[:, None] == jnp.arange(row_tiles, dtype=jnp.int32)[None, :]).astype(jnp.float32)

    def sources_of(gathered):
        f = gathered.reshape(nblocks, vecs, row_tiles, TILE)
        return f[b_of, :, t_of, :]

    def total_squares(gathered):
        return jnp.sum(gathered.reshape(nblocks, vecs)[p_of], axis=0)

    def apply_sources(sources):
        src_hi_f = lax.reduce_precision(sources, exponent_bits=8, mantissa_bits=7)
        src_hi = src_hi_f.astype(jnp.bfloat16)
        src_lo = (sources - src_hi_f).astype(jnp.bfloat16)
        both = jnp.concatenate([src_hi, src_lo], axis=1)
        p_hi = jnp.einsum("kvc,krc->kvr", both, tiles_hi, preferred_element_type=jnp.float32)
        p_lo = jnp.einsum("kvc,krc->kvr", src_hi, tiles_lo, preferred_element_type=jnp.float32)
        product = (p_hi[:, :vecs] + p_hi[:, vecs:]) + p_lo
        total = jnp.einsum("kvr,kt->vtr", product, onehot, precision=lax.Precision.HIGHEST)
        return total.reshape(vecs, width)

    def scaled(field):
        (gathered,) = plane_gather([field])
        out = apply_sources(sources_of(gathered))
        return (out - center[0] * field) / halfwidth[0]

    current = vectors
    third = None
    partial = None
    for step in range(PASSES):
        if step == 0:
            first = scaled(current)
        else:
            gathered, sq = plane_gather([third, partial])
            squares = total_squares(sq)
            norm = jnp.sqrt(squares / total_rows + 1e-06)
            current = third / norm[:, None]
            sources = sources_of(gathered) / norm[None, :, None]
            first = (apply_sources(sources) - center[0] * current) / halfwidth[0]
        second = 2.0 * scaled(first) - current
        third = 2.0 * scaled(second) - first
        partial = jnp.sum(third * third, axis=1)[:, None]
    (sq,) = plane_gather([partial])
    squares = total_squares(sq)
    return third / jnp.sqrt(squares / total_rows + 1e-06)[:, None]


def solution(mesh):
    return jax.shard_map(
        shards,
        mesh=mesh,
        in_specs=(
            P("bulk", ("blk", "reader")),
            P(("blk", "reader"), None, None, None, None),
            P(("blk", "reader"), None, None),
            P(("blk", "reader"), None, None),
            P(),
            P(),
        ),
        out_specs=P("bulk", ("blk", "reader")),
        check_vma=False,
    )
```

```python
import jax
import jax.numpy as jnp
from jax import lax
from jax.sharding import PartitionSpec as P

TILE = 128
PASSES = 2
AXES = ("blk", "reader")
RING = 4


def device_index(core, y, x):
    return ((y // 2) * 2 + core) * 8 + (y % 2) * 4 + x


def shift_perm(step, first_axis_by_core):
    pairs = []
    for core in range(2):
        axis = first_axis_by_core[core]
        for y in range(RING):
            for x in range(RING):
                if axis == "x":
                    dst = device_index(core, y, (x + step) % RING)
                else:
                    dst = device_index(core, (y + step) % RING, x)
                pairs.append((device_index(core, y, x), dst))
    return pairs


def core_swap_perm():
    pairs = []
    for core in range(2):
        for y in range(RING):
            for x in range(RING):
                pairs.append((device_index(core, y, x), device_index(1 - core, y, x)))
    return pairs


def direct_round(leaves, axis_by_core):
    got = [lax.ppermute(leaves, AXES, shift_perm(RING - step, axis_by_core)) for step in (1, 2, 3)]
    return [jnp.stack([own, a, b, c], axis=0) for own, a, b, c in zip(leaves, *got)]


def plane_gather(leaves):
    stage1 = direct_round(leaves, ("x", "y"))
    early = lax.ppermute(stage1, AXES, core_swap_perm())
    stage2 = direct_round(stage1, ("y", "x"))
    late = lax.ppermute([t[1:] for t in stage2], AXES, core_swap_perm())
    other = [jnp.concatenate([e[None], l], axis=0) for e, l in zip(early, late)]
    out = []
    for s, o in zip(stage2, other):
        both = jnp.concatenate([s.reshape((RING * RING,) + s.shape[2:]), o.reshape((RING * RING,) + o.shape[2:])], axis=0)
        out.append(both)
    return out


def layout_index(q_index, x0, y0, core):
    blk = q_index // 8
    reader = q_index % 8
    cc = blk % 2
    y = (blk // 2) * 2 + reader // 4
    x = reader % 4
    dy = (y - y0) % RING
    dx = (x - x0) % RING
    chip = jnp.where(cc == 0, dy * 4 + dx, dx * 4 + dy)
    return jnp.where(cc == core, 0, RING * RING) + chip


def shards(vectors, ham_tiles, tile_rows, tile_cols, center, halfwidth):
    tiles_here = ham_tiles[0]
    rows_here = tile_rows[0]
    cols_here = tile_cols[0]
    vecs = vectors.shape[0]
    width = vectors.shape[1]
    row_tiles = width // TILE
    groups = tiles_here.shape[0]
    slots = tiles_here.shape[1]
    nblocks = lax.axis_size("blk") * lax.axis_size("reader")
    total_rows = width * nblocks
    group_tiles = lax.axis_size("reader") * row_tiles

    reader = lax.axis_index("reader")
    blk = lax.axis_index("blk")
    x0 = reader % 4
    y0 = (blk // 2) * 2 + reader // 4

    offsets = (jnp.arange(groups, dtype=jnp.int32) * group_tiles)[:, None]
    glob = (offsets + cols_here).reshape(-1)
    q_of = glob // row_tiles
    t_of = glob % row_tiles
    core = blk % 2
    b_of = layout_index(q_of, x0, y0, core)
    all_q = jnp.arange(nblocks, dtype=jnp.int32)
    p_of = layout_index(all_q, x0, y0, core)

    tiles = tiles_here.reshape(groups * slots, TILE, TILE)
    rows = rows_here.reshape(-1)
    onehot = (rows[:, None] == jnp.arange(row_tiles, dtype=jnp.int32)[None, :]).astype(jnp.float32)

    def sources_of(gathered):
        f = gathered.reshape(nblocks, vecs, row_tiles, TILE)
        return f[b_of, :, t_of, :]

    def total_squares(gathered):
        return jnp.sum(gathered.reshape(nblocks, vecs)[p_of], axis=0)

    def apply_sources(sources):
        product = jnp.einsum("kvc,krc->kvr", sources, tiles, precision=lax.Precision.HIGH)
        total = jnp.einsum("kvr,kt->vtr", product, onehot, precision=lax.Precision.HIGHEST)
        return total.reshape(vecs, width)

    def scaled(field):
        (gathered,) = plane_gather([field])
        out = apply_sources(sources_of(gathered))
        return (out - center[0] * field) / halfwidth[0]

    current = vectors
    third = None
    partial = None
    for step in range(PASSES):
        if step == 0:
            first = scaled(current)
        else:
            gathered, sq = plane_gather([third, partial])
            squares = total_squares(sq)
            norm = jnp.sqrt(squares / total_rows + 1e-06)
            current = third / norm[:, None]
            sources = sources_of(gathered) / norm[None, :, None]
            first = (apply_sources(sources) - center[0] * current) / halfwidth[0]
        second = 2.0 * scaled(first) - current
        third = 2.0 * scaled(second) - first
        partial = jnp.sum(third * third, axis=1)[:, None]
    (sq,) = plane_gather([partial])
    squares = total_squares(sq)
    return third / jnp.sqrt(squares / total_rows + 1e-06)[:, None]


def solution(mesh):
    return jax.shard_map(
        shards,
        mesh=mesh,
        in_specs=(
            P("bulk", ("blk", "reader")),
            P(("blk", "reader"), None, None, None, None),
            P(("blk", "reader"), None, None),
            P(("blk", "reader"), None, None),
            P(),
            P(),
        ),
        out_specs=P("bulk", ("blk", "reader")),
        check_vma=False,
    )
```

```python
import jax
import jax.numpy as jnp
from jax import lax
from jax.sharding import PartitionSpec as P

TILE = 128
PASSES = 2
AXES = ("blk", "reader")
RING = 4


def device_index(core, y, x):
    return ((y // 2) * 2 + core) * 8 + (y % 2) * 4 + x


def shift_perm(step, first_axis_by_core):
    pairs = []
    for core in range(2):
        axis = first_axis_by_core[core]
        for y in range(RING):
            for x in range(RING):
                if axis == "x":
                    dst = device_index(core, y, (x + step) % RING)
                else:
                    dst = device_index(core, (y + step) % RING, x)
                pairs.append((device_index(core, y, x), dst))
    return pairs


def core_swap_perm():
    pairs = []
    for core in range(2):
        for y in range(RING):
            for x in range(RING):
                pairs.append((device_index(core, y, x), device_index(1 - core, y, x)))
    return pairs


def direct_round(leaves, axis_by_core):
    got = [lax.ppermute(leaves, AXES, shift_perm(RING - step, axis_by_core)) for step in (1, 2, 3)]
    return [jnp.stack([own, a, b, c], axis=0) for own, a, b, c in zip(leaves, *got)]


def plane_gather(leaves):
    stage1 = direct_round(leaves, ("x", "y"))
    early = lax.ppermute(stage1, AXES, core_swap_perm())
    stage2 = direct_round(stage1, ("y", "x"))
    late = [lax.ppermute([t[i] for t in stage2], AXES, core_swap_perm()) for i in range(1, RING)]
    other = [jnp.stack([e] + [l[j] for l in late], axis=0) for j, e in enumerate(early)]
    out = []
    for s, o in zip(stage2, other):
        both = jnp.concatenate([s.reshape((RING * RING,) + s.shape[2:]), o.reshape((RING * RING,) + o.shape[2:])], axis=0)
        out.append(both)
    return out


def layout_index(q_index, x0, y0, core):
    blk = q_index // 8
    reader = q_index % 8
    cc = blk % 2
    y = (blk // 2) * 2 + reader // 4
    x = reader % 4
    dy = (y - y0) % RING
    dx = (x - x0) % RING
    chip = jnp.where(cc == 0, dy * 4 + dx, dx * 4 + dy)
    return jnp.where(cc == core, 0, RING * RING) + chip


def shards(vectors, ham_tiles, tile_rows, tile_cols, center, halfwidth):
    tiles_here = ham_tiles[0]
    rows_here = tile_rows[0]
    cols_here = tile_cols[0]
    vecs = vectors.shape[0]
    width = vectors.shape[1]
    row_tiles = width // TILE
    groups = tiles_here.shape[0]
    slots = tiles_here.shape[1]
    nblocks = lax.axis_size("blk") * lax.axis_size("reader")
    total_rows = width * nblocks
    group_tiles = lax.axis_size("reader") * row_tiles

    reader = lax.axis_index("reader")
    blk = lax.axis_index("blk")
    x0 = reader % 4
    y0 = (blk // 2) * 2 + reader // 4

    offsets = (jnp.arange(groups, dtype=jnp.int32) * group_tiles)[:, None]
    glob = (offsets + cols_here).reshape(-1)
    q_of = glob // row_tiles
    t_of = glob % row_tiles
    core = blk % 2
    b_of = layout_index(q_of, x0, y0, core)
    all_q = jnp.arange(nblocks, dtype=jnp.int32)
    p_of = layout_index(all_q, x0, y0, core)

    tiles = tiles_here.reshape(groups * slots, TILE, TILE)
    rows = rows_here.reshape(-1)
    onehot = (rows[:, None] == jnp.arange(row_tiles, dtype=jnp.int32)[None, :]).astype(jnp.float32)

    def sources_of(gathered):
        f = gathered.reshape(nblocks, vecs, row_tiles, TILE)
        return f[b_of, :, t_of, :]

    def total_squares(gathered):
        return jnp.sum(gathered.reshape(nblocks, vecs)[p_of], axis=0)

    def apply_sources(sources):
        product = jnp.einsum("kvc,krc->kvr", sources, tiles, precision=lax.Precision.HIGH)
        total = jnp.einsum("kvr,kt->vtr", product, onehot, precision=lax.Precision.HIGHEST)
        return total.reshape(vecs, width)

    def scaled(field):
        (gathered,) = plane_gather([field])
        out = apply_sources(sources_of(gathered))
        return (out - center[0] * field) / halfwidth[0]

    current = vectors
    third = None
    partial = None
    for step in range(PASSES):
        if step == 0:
            first = scaled(current)
        else:
            gathered, sq = plane_gather([third, partial])
            squares = total_squares(sq)
            norm = jnp.sqrt(squares / total_rows + 1e-06)
            current = third / norm[:, None]
            sources = sources_of(gathered) / norm[None, :, None]
            first = (apply_sources(sources) - center[0] * current) / halfwidth[0]
        second = 2.0 * scaled(first) - current
        third = 2.0 * scaled(second) - first
        partial = jnp.sum(third * third, axis=1)[:, None]
    (sq,) = plane_gather([partial])
    squares = total_squares(sq)
    return third / jnp.sqrt(squares / total_rows + 1e-06)[:, None]


def solution(mesh):
    return jax.shard_map(
        shards,
        mesh=mesh,
        in_specs=(
            P("bulk", ("blk", "reader")),
            P(("blk", "reader"), None, None, None, None),
            P(("blk", "reader"), None, None),
            P(("blk", "reader"), None, None),
            P(),
            P(),
        ),
        out_specs=P("bulk", ("blk", "reader")),
        check_vma=False,
    )
```

```python
import jax
import jax.numpy as jnp
from jax import lax
from jax.sharding import PartitionSpec as P

TILE = 128
PASSES = 2
AXES = ("blk", "reader")
RING = 4


def device_index(core, y, x):
    return ((y // 2) * 2 + core) * 8 + (y % 2) * 4 + x


def shift_perm(step, first_axis_by_core):
    pairs = []
    for core in range(2):
        axis = first_axis_by_core[core]
        for y in range(RING):
            for x in range(RING):
                if axis == "x":
                    dst = device_index(core, y, (x + step) % RING)
                else:
                    dst = device_index(core, (y + step) % RING, x)
                pairs.append((device_index(core, y, x), dst))
    return pairs


def core_swap_perm():
    pairs = []
    for core in range(2):
        for y in range(RING):
            for x in range(RING):
                pairs.append((device_index(core, y, x), device_index(1 - core, y, x)))
    return pairs


def direct_round(leaves, axis_by_core):
    got = [lax.ppermute(leaves, AXES, shift_perm(RING - step, axis_by_core)) for step in (1, 2, 3)]
    return [jnp.stack([own, a, b, c], axis=0) for own, a, b, c in zip(leaves, *got)]


def plane_gather(leaves):
    stage1 = direct_round(leaves, ("x", "y"))
    early = lax.ppermute(stage1, AXES, core_swap_perm())
    stage2 = direct_round(stage1, ("y", "x"))
    late = []
    for i in range(1, RING):
        lo = lax.ppermute([t[i, : RING // 2] for t in stage2], AXES, core_swap_perm())
        hi = lax.ppermute([t[i, RING // 2 :] for t in stage2], AXES, core_swap_perm())
        late.append([jnp.concatenate([a, b], axis=0) for a, b in zip(lo, hi)])
    other = [jnp.stack([e] + [l[j] for l in late], axis=0) for j, e in enumerate(early)]
    out = []
    for s, o in zip(stage2, other):
        both = jnp.concatenate([s.reshape((RING * RING,) + s.shape[2:]), o.reshape((RING * RING,) + o.shape[2:])], axis=0)
        out.append(both)
    return out


def layout_index(q_index, x0, y0, core):
    blk = q_index // 8
    reader = q_index % 8
    cc = blk % 2
    y = (blk // 2) * 2 + reader // 4
    x = reader % 4
    dy = (y - y0) % RING
    dx = (x - x0) % RING
    chip = jnp.where(cc == 0, dy * 4 + dx, dx * 4 + dy)
    return jnp.where(cc == core, 0, RING * RING) + chip


def shards(vectors, ham_tiles, tile_rows, tile_cols, center, halfwidth):
    tiles_here = ham_tiles[0]
    rows_here = tile_rows[0]
    cols_here = tile_cols[0]
    vecs = vectors.shape[0]
    width = vectors.shape[1]
    row_tiles = width // TILE
    groups = tiles_here.shape[0]
    slots = tiles_here.shape[1]
    nblocks = lax.axis_size("blk") * lax.axis_size("reader")
    total_rows = width * nblocks
    group_tiles = lax.axis_size("reader") * row_tiles

    reader = lax.axis_index("reader")
    blk = lax.axis_index("blk")
    x0 = reader % 4
    y0 = (blk // 2) * 2 + reader // 4

    offsets = (jnp.arange(groups, dtype=jnp.int32) * group_tiles)[:, None]
    glob = (offsets + cols_here).reshape(-1)
    q_of = glob // row_tiles
    t_of = glob % row_tiles
    core = blk % 2
    b_of = layout_index(q_of, x0, y0, core)
    all_q = jnp.arange(nblocks, dtype=jnp.int32)
    p_of = layout_index(all_q, x0, y0, core)

    tiles = tiles_here.reshape(groups * slots, TILE, TILE)
    rows = rows_here.reshape(-1)
    onehot = (rows[:, None] == jnp.arange(row_tiles, dtype=jnp.int32)[None, :]).astype(jnp.float32)

    def sources_of(gathered):
        f = gathered.reshape(nblocks, vecs, row_tiles, TILE)
        return f[b_of, :, t_of, :]

    def total_squares(gathered):
        return jnp.sum(gathered.reshape(nblocks, vecs)[p_of], axis=0)

    def apply_sources(sources):
        product = jnp.einsum("kvc,krc->kvr", sources, tiles, precision=lax.Precision.HIGH)
        total = jnp.einsum("kvr,kt->vtr", product, onehot, precision=lax.Precision.HIGHEST)
        return total.reshape(vecs, width)

    def scaled(field):
        (gathered,) = plane_gather([field])
        out = apply_sources(sources_of(gathered))
        return (out - center[0] * field) / halfwidth[0]

    current = vectors
    third = None
    partial = None
    for step in range(PASSES):
        if step == 0:
            first = scaled(current)
        else:
            gathered, sq = plane_gather([third, partial])
            squares = total_squares(sq)
            norm = jnp.sqrt(squares / total_rows + 1e-06)
            current = third / norm[:, None]
            sources = sources_of(gathered) / norm[None, :, None]
            first = (apply_sources(sources) - center[0] * current) / halfwidth[0]
        second = 2.0 * scaled(first) - current
        third = 2.0 * scaled(second) - first
        partial = jnp.sum(third * third, axis=1)[:, None]
    (sq,) = plane_gather([partial])
    squares = total_squares(sq)
    return third / jnp.sqrt(squares / total_rows + 1e-06)[:, None]


def solution(mesh):
    return jax.shard_map(
        shards,
        mesh=mesh,
        in_specs=(
            P("bulk", ("blk", "reader")),
            P(("blk", "reader"), None, None, None, None),
            P(("blk", "reader"), None, None),
            P(("blk", "reader"), None, None),
            P(),
            P(),
        ),
        out_specs=P("bulk", ("blk", "reader")),
        check_vma=False,
    )
```

```python
import jax
import jax.numpy as jnp
from jax import lax
from jax.sharding import PartitionSpec as P

TILE = 128
PASSES = 2
AXES = ("blk", "reader")
RING = 4


def device_index(core, y, x):
    return ((y // 2) * 2 + core) * 8 + (y % 2) * 4 + x


def shift_perm(step, first_axis_by_core):
    pairs = []
    for core in range(2):
        axis = first_axis_by_core[core]
        for y in range(RING):
            for x in range(RING):
                if axis == "x":
                    dst = device_index(core, y, (x + step) % RING)
                else:
                    dst = device_index(core, (y + step) % RING, x)
                pairs.append((device_index(core, y, x), dst))
    return pairs


def core_swap_perm():
    pairs = []
    for core in range(2):
        for y in range(RING):
            for x in range(RING):
                pairs.append((device_index(core, y, x), device_index(1 - core, y, x)))
    return pairs


def direct_round(leaves, axis_by_core):
    got = [lax.ppermute(leaves, AXES, shift_perm(RING - step, axis_by_core)) for step in (1, 2, 3)]
    return [jnp.stack([own, a, b, c], axis=0) for own, a, b, c in zip(leaves, *got)]


def plane_gather(leaves, split_swap=True):
    stage1 = direct_round(leaves, ("x", "y"))
    if split_swap:
        early = lax.ppermute(stage1, AXES, core_swap_perm())
        stage2 = direct_round(stage1, ("y", "x"))
        late = [lax.ppermute([t[i] for t in stage2], AXES, core_swap_perm()) for i in range(1, RING)]
        other = [jnp.stack([e] + [l[j] for l in late], axis=0) for j, e in enumerate(early)]
    else:
        stage2 = direct_round(stage1, ("y", "x"))
        other = lax.ppermute(stage2, AXES, core_swap_perm())
    out = []
    for s, o in zip(stage2, other):
        both = jnp.concatenate([s.reshape((RING * RING,) + s.shape[2:]), o.reshape((RING * RING,) + o.shape[2:])], axis=0)
        out.append(both)
    return out


def layout_index(q_index, x0, y0, core):
    blk = q_index // 8
    reader = q_index % 8
    cc = blk % 2
    y = (blk // 2) * 2 + reader // 4
    x = reader % 4
    dy = (y - y0) % RING
    dx = (x - x0) % RING
    chip = jnp.where(cc == 0, dy * 4 + dx, dx * 4 + dy)
    return jnp.where(cc == core, 0, RING * RING) + chip


def shards(vectors, ham_tiles, tile_rows, tile_cols, center, halfwidth):
    tiles_here = ham_tiles[0]
    rows_here = tile_rows[0]
    cols_here = tile_cols[0]
    vecs = vectors.shape[0]
    width = vectors.shape[1]
    row_tiles = width // TILE
    groups = tiles_here.shape[0]
    slots = tiles_here.shape[1]
    nblocks = lax.axis_size("blk") * lax.axis_size("reader")
    total_rows = width * nblocks
    group_tiles = lax.axis_size("reader") * row_tiles

    reader = lax.axis_index("reader")
    blk = lax.axis_index("blk")
    x0 = reader % 4
    y0 = (blk // 2) * 2 + reader // 4

    offsets = (jnp.arange(groups, dtype=jnp.int32) * group_tiles)[:, None]
    glob = (offsets + cols_here).reshape(-1)
    q_of = glob // row_tiles
    t_of = glob % row_tiles
    core = blk % 2
    b_of = layout_index(q_of, x0, y0, core)
    all_q = jnp.arange(nblocks, dtype=jnp.int32)
    p_of = layout_index(all_q, x0, y0, core)

    tiles = tiles_here.reshape(groups * slots, TILE, TILE)
    rows = rows_here.reshape(-1)
    onehot = (rows[:, None] == jnp.arange(row_tiles, dtype=jnp.int32)[None, :]).astype(jnp.float32)

    def sources_of(gathered):
        f = gathered.reshape(nblocks, vecs, row_tiles, TILE)
        return f[b_of, :, t_of, :]

    def total_squares(gathered):
        return jnp.sum(gathered.reshape(nblocks, vecs)[p_of], axis=0)

    def apply_sources(sources):
        product = jnp.einsum("kvc,krc->kvr", sources, tiles, precision=lax.Precision.HIGH)
        total = jnp.einsum("kvr,kt->vtr", product, onehot, precision=lax.Precision.HIGHEST)
        return total.reshape(vecs, width)

    def scaled(field):
        (gathered,) = plane_gather([field])
        out = apply_sources(sources_of(gathered))
        return (out - center[0] * field) / halfwidth[0]

    current = vectors
    third = None
    partial = None
    for step in range(PASSES):
        if step == 0:
            first = scaled(current)
        else:
            gathered, sq = plane_gather([third, partial])
            squares = total_squares(sq)
            norm = jnp.sqrt(squares / total_rows + 1e-06)
            current = third / norm[:, None]
            sources = sources_of(gathered) / norm[None, :, None]
            first = (apply_sources(sources) - center[0] * current) / halfwidth[0]
        second = 2.0 * scaled(first) - current
        third = 2.0 * scaled(second) - first
        partial = jnp.sum(third * third, axis=1)[:, None]
    (sq,) = plane_gather([partial], split_swap=False)
    squares = total_squares(sq)
    return third / jnp.sqrt(squares / total_rows + 1e-06)[:, None]


def solution(mesh):
    return jax.shard_map(
        shards,
        mesh=mesh,
        in_specs=(
            P("bulk", ("blk", "reader")),
            P(("blk", "reader"), None, None, None, None),
            P(("blk", "reader"), None, None),
            P(("blk", "reader"), None, None),
            P(),
            P(),
        ),
        out_specs=P("bulk", ("blk", "reader")),
        check_vma=False,
    )
```
